256 devices in a mesh: leaf: 4 (over z_hi), row: 8 (over z_lo, y), col: 8 (over x, core).
Axes of the slice: x: 4, y: 4, z: 8 (z_hi: 4, z_lo: 2; z = z_hi * 2 + z_lo), core: 2. Of those that a mesh axis runs over, the one named last changes fastest.
Arguments:
- lanczos_low: float32 [4, 8, 8, 128, 256], P('leaf', 'col', 'row'), may hold values from -6 to 6
- lanczos_mid: float32 [4, 8, 8, 96, 256], P('leaf', 'col', 'row'), may hold values from -6 to 6
- lanczos_top: float32 [4, 8, 8, 64, 256], P('leaf', 'col', 'row'), may hold values from -6 to 6
- pivot_low: bfloat16 [4, 8192, 8192], P('leaf', 'row', 'col'), as said below
- update_low: bfloat16 [4, 8192, 8192], P('leaf', 'row', 'col'), may hold values from -0.0625 to 0.0625
- pivot_mid: bfloat16 [12288, 24576], P('row', ('leaf', 'col'))
- update_mid: bfloat16 [12288, 16384], P('row', ('leaf', 'col')), may hold values from -0.0546875 to 0.0546875
- pivot_top: bfloat16 [16384, 16384], P('row', ('leaf', 'col'))
- rows_low: int32 [4, 8, 8, 2, 64], P('leaf', 'col', 'row'), may hold values from 0 to 20479, as said below
- rows_mid: int32 [4, 8, 8, 4, 16], P('leaf', 'col', 'row'), may hold values from 0 to 16383, as said below
Outputs:
- solved_low: float32 [4, 8, 8, 128, 256], P('leaf', 'col', 'row')
- solved_mid: float32 [4, 8, 8, 96, 256], P('leaf', 'col', 'row')
- solved_top: float32 [4, 8, 8, 64, 256], P('leaf', 'col', 'row')
The draws below stay inside these ranges and needn't reach their ends.
Inputs may be any that keep to these rules, and one draw needn't show every extreme that they name: rows_low[2h + a, c, r, s, t] over t are distinct rows of front h, all among pivot rows a 6144 + (c * 8 + r) * 96 + k (0 <= k < 96) and update rows 12288 + a 4096 + (c * 8 + r) * 64 + k (0 <= k < 64); for s = 0 they include the first of those pivot rows and the last of those update rows. rows_mid[q, c, r, 2h + s, t] over s and t are distinct root rows q * 4096 + (c * 8 + r) * 64 + k (0 <= k < 64); for h = 0 they include the first and the last of them. pivot_low, pivot_mid's two square halves and pivot_top are lower triangular.
All inputs are finite; a program needn't handle non-finite values.
Results may differ from the reference program's by a relative error of at most 0.023.
Values may be sent and summed in bfloat16 or wider, within the bound.
No kernel may reach another device: no remote copies, remote signals or barrier semaphores. Data moves between devices by JAX's collectives and lax.ppermute only.
A program may use at most 64 MiB of HBM per device.

```python
import math
import jax
import jax.numpy as jnp
from jax import lax

R = 256
P2 = 8192
E2 = 8192
P1 = 12288
E1 = 8192
P0 = 16384
PL2 = 128
CH2 = 64
PL1 = 96
UL1 = 64
CH1 = 16
PL0 = 64
N_LEAF = 4
N_ROW = 8
N_COL = 8


def lower_inverse(key, shape, width):
    first_key, second_key = jax.random.split(jax.random.fold_in(key, 7))
    row_ids = lax.broadcasted_iota(jnp.int32, shape, len(shape) - 2)
    col_ids = lax.broadcasted_iota(jnp.int32, shape, len(shape) - 1) % width
    diag_shape = shape[:-2] + (1, shape[-1])
    lower_part = jax.random.normal(first_key, shape, jnp.float32) * (0.6 / math.sqrt(width))
    diag_part = jnp.exp(jax.random.uniform(second_key, diag_shape, jnp.float32, math.log(0.6), math.log(1.6)))
    values = jnp.where(col_ids < row_ids, lower_part, jnp.where(col_ids == row_ids, diag_part, 0.0))
    return values.astype(jnp.bfloat16)


def draw_pivot_low(key, part):
    return lower_inverse(key, (N_LEAF, P2, P2), P2)


def draw_pivot_mid(key, part):
    return lower_inverse(jax.random.fold_in(key, 3), (P1, 2 * P1), P1)


def draw_pivot_top(key, part):
    return lower_inverse(jax.random.fold_in(key, 5), (P0, P0), P0)


def pick_slots(key, total_slots, picked, forced):
    first_key, second_key, third_key = jax.random.split(key, 3)
    drawn_pick = jax.random.permutation(first_key, total_slots)[:picked].astype(jnp.int32)
    inner_pick = 1 + jax.random.permutation(second_key, total_slots - 2)[:picked - 2].astype(jnp.int32)
    end_slots = jnp.array([0, total_slots - 1], dtype=jnp.int32)
    forced_pick = jax.random.permutation(third_key, jnp.concatenate([end_slots, inner_pick]))
    return jnp.where(forced, forced_pick, drawn_pick)


def draw_rows_low(key, part):
    blocks_count = N_LEAF * N_COL * N_ROW * 2
    block_keys = jax.random.split(jax.random.fold_in(key, 11), blocks_count)
    forced_flags = jnp.arange(blocks_count) % 2 == 0
    chosen = jax.vmap(lambda one_key, one_flag: pick_slots(one_key, PL1 + UL1, CH2, one_flag))(block_keys, forced_flags)
    chosen = chosen.reshape(N_LEAF, N_COL, N_ROW, 2, CH2)
    leaf_ids = lax.broadcasted_iota(jnp.int32, chosen.shape, 0)
    col_ids = lax.broadcasted_iota(jnp.int32, chosen.shape, 1)
    row_ids = lax.broadcasted_iota(jnp.int32, chosen.shape, 2)
    pair_half = leaf_ids % 2
    position = col_ids * N_ROW + row_ids
    pivot_rows = pair_half * (P1 // 2) + position * PL1 + chosen
    update_rows = P1 + pair_half * (E1 // 2) + position * UL1 + chosen - PL1
    return jnp.where(chosen < PL1, pivot_rows, update_rows).astype(jnp.int32)


def draw_rows_mid(key, part):
    blocks_count = N_LEAF * N_COL * N_ROW * 2
    block_keys = jax.random.split(jax.random.fold_in(key, 13), blocks_count)
    forced_flags = jnp.arange(blocks_count) % 2 == 0
    chosen = jax.vmap(lambda one_key, one_flag: pick_slots(one_key, PL0, 2 * CH1, one_flag))(block_keys, forced_flags)
    chosen = chosen.reshape(N_LEAF, N_COL, N_ROW, 2, 2, CH1).reshape(N_LEAF, N_COL, N_ROW, 4, CH1)
    leaf_ids = lax.broadcasted_iota(jnp.int32, chosen.shape, 0)
    col_ids = lax.broadcasted_iota(jnp.int32, chosen.shape, 1)
    row_ids = lax.broadcasted_iota(jnp.int32, chosen.shape, 2)
    return (leaf_ids * (P0 // 4) + (col_ids * N_ROW + row_ids) * PL0 + chosen).astype(jnp.int32)


def block_levels(rng, dims, cuts, smallest, high):
    def one(axis_at, parts):
        draws = jax.random.uniform(jax.random.fold_in(jax.random.fold_in(rng, 6), axis_at), (parts,), jnp.float32, smallest / len(cuts), high / len(cuts))
        return jnp.repeat(jnp.exp(draws), dims[axis_at] // parts).reshape((-1,) + (1,) * (len(dims) - axis_at - 1))

    loudness = one(*cuts[0])
    for cut in cuts[1:]:
        loudness = loudness * one(*cut)
    return loudness


def gaussian(rng, extent, spread, limit, shards=(), kind=jnp.bfloat16):
    entries = spread * jax.random.normal(rng, extent, jnp.float32)
    if shards:
        entries = entries * block_levels(rng, extent, shards, -0.22, 0.18)
    return jnp.clip(entries, -limit, limit).astype(kind)


def setup_inputs(seed: int = 0) -> dict:
    keys = jax.random.split(jax.random.key(seed), 11)
    return {
        "lanczos_low": gaussian(keys[0], (N_LEAF, N_COL, N_ROW, PL2, R), 1.0, 6.0, ((0, 4), (1, 8), (2, 8)), jnp.float32),
        "lanczos_mid": gaussian(keys[1], (N_LEAF, N_COL, N_ROW, PL1, R), 1.0, 6.0, ((0, 4), (1, 8), (2, 8)), jnp.float32),
        "lanczos_top": gaussian(keys[2], (N_LEAF, N_COL, N_ROW, PL0, R), 1.0, 6.0, ((0, 4), (1, 8), (2, 8)), jnp.float32),
        "pivot_low": draw_pivot_low(jax.random.fold_in(keys[10], 71), 0),
        "update_low": gaussian(keys[4], (N_LEAF, P2, E2), P2 ** -0.5, 0.0625, ((0, 4), (1, 8), (2, 8))),
        "pivot_mid": draw_pivot_mid(jax.random.fold_in(keys[10], 71), 0),
        "update_mid": gaussian(keys[6], (P1, 2 * E1), P1 ** -0.5, 0.0546875, ((0, 8), (1, 32))),
        "pivot_top": draw_pivot_top(jax.random.fold_in(keys[10], 71), 0),
        "rows_low": draw_rows_low(jax.random.fold_in(keys[10], 71), 0),
        "rows_mid": draw_rows_mid(jax.random.fold_in(keys[10], 71), 0),
    }


def bf_product(matrix, vector):
    return jnp.dot(matrix, vector.astype(jnp.bfloat16), preferred_element_type=jnp.float32)


def reference(lanczos_low, lanczos_mid, lanczos_top, pivot_low, update_low, pivot_mid, update_mid, pivot_top, rows_low, rows_mid):
    rhs_width = lanczos_low.shape[-1]
    low_in = lanczos_low.reshape(4, P2, rhs_width)
    mid_in = lanczos_mid.reshape(2, P1, rhs_width)
    top_in = lanczos_top.reshape(P0, rhs_width)
    low_map = rows_low.reshape(2, 2, N_COL, N_ROW, 2, CH2).transpose(0, 4, 2, 3, 1, 5).reshape(4, E2)
    mid_map = rows_mid.transpose(3, 1, 2, 0, 4).reshape(2, E1)
    low_y = []
    low_c = []
    for front_id in range(4):
        solved = bf_product(pivot_low[front_id], low_in[front_id])
        low_y.append(solved)
        low_c.append(bf_product(update_low[front_id].T, solved))
    mid_y = []
    top_front = top_in
    for parent in range(2):
        pivots = pivot_mid[:, parent * P1:(parent + 1) * P1]
        updates = update_mid[:, parent * E1:(parent + 1) * E1]
        front_rows = jnp.concatenate([mid_in[parent], jnp.zeros((E1, rhs_width), mid_in.dtype)], 0)
        for child in range(2):
            front_rows = front_rows.at[low_map[2 * parent + child]].add(-low_c[2 * parent + child])
        solved = bf_product(pivots, front_rows[:P1])
        mid_y.append(solved)
        passed = front_rows[P1:] - bf_product(updates.T, solved)
        top_front = top_front.at[mid_map[parent]].add(passed)
    top_y = bf_product(pivot_top, top_front)
    top_x = bf_product(pivot_top.T, top_y)
    mid_x = []
    parent_values = []
    for parent in range(2):
        pivots = pivot_mid[:, parent * P1:(parent + 1) * P1]
        updates = update_mid[:, parent * E1:(parent + 1) * E1]
        above = top_x[mid_map[parent]]
        reduced = mid_y[parent] - bf_product(updates, above)
        solved = bf_product(pivots.T, reduced)
        mid_x.append(solved)
        parent_values.append(jnp.concatenate([solved, above], 0))
    low_x = []
    for front_id in range(4):
        above = parent_values[front_id // 2][low_map[front_id]]
        reduced = low_y[front_id] - bf_product(update_low[front_id], above)
        low_x.append(bf_product(pivot_low[front_id].T, reduced))
    solved_low = jnp.stack(low_x).reshape(lanczos_low.shape)
    solved_mid = jnp.stack(mid_x).reshape(lanczos_mid.shape)
    solved_top = top_x.reshape(lanczos_top.shape)
    return (solved_low, solved_mid, solved_top)
```

```python
import jax
import jax.numpy as jnp
from jax import lax
from jax.sharding import PartitionSpec as P

P1 = 12288


def from_partner(block, axis, bit):
    count = lax.axis_size(axis)
    route = []
    for low in range(count):
        high = low | 1 << bit
        if high != low and high < count:
            route += [(low, high), (high, low)]
    return lax.ppermute(block, axis, route)


def partner(block_data, leaf_bit):
    return from_partner(block_data.astype(jnp.bfloat16), "leaf", leaf_bit).astype(block_data.dtype)


def scatter_sum(block, axis, send_dtype):
    count = lax.axis_size(axis)
    pieces = block.astype(send_dtype).reshape(count, -1, block.shape[-1])
    pieces = lax.all_to_all(pieces, axis, 0, 0, tiled=True)
    return pieces.astype(jnp.float32).sum(0)


def gather_rows(block, axis):
    count = lax.axis_size(axis)
    copies = jnp.broadcast_to(block[None], (count,) + block.shape)
    return lax.all_to_all(copies, axis, 0, 0, tiled=True).reshape(-1, block.shape[-1])


def forward_apply(matrix, vector, leaf_bits):
    gathered = gather_rows(vector, "row")
    result = scatter_sum(
        jnp.dot(matrix, gathered, preferred_element_type=jnp.float32), "col", jnp.float32
    )
    for leaf_bit in leaf_bits:
        result = result + partner(result, leaf_bit)
    return result


def reverse_apply(matrix, vector):
    gathered = gather_rows(vector, "col")
    return scatter_sum(
        lax.dot_general(
            matrix, gathered, (((0,), (0,)), ((), ())), preferred_element_type=jnp.float32
        ),
        "row",
        jnp.bfloat16,
    )


def parent_slot(parent_rows, pivot_local, update_local):
    return jnp.where(
        parent_rows < P1, parent_rows % pivot_local, pivot_local + (parent_rows - P1) % update_local
    )


def pick_span(spans, index_value):
    return lax.dynamic_index_in_dim(spans, index_value, 0, keepdims=False)


def body(
    lanczos_low,
    lanczos_mid,
    lanczos_top,
    pivot_low,
    update_low,
    pivot_mid,
    update_mid,
    pivot_top,
    rows_low,
    rows_mid,
):
    rhs_width = lanczos_low.shape[-1]
    low_in = lanczos_low.reshape(-1, rhs_width)
    mid_in = lanczos_mid.reshape(-1, rhs_width)
    top_in = lanczos_top.reshape(-1, rhs_width)
    pivot_local_low = pivot_low[0]
    update_local_low = update_low[0]
    pivot_local = mid_in.shape[0]
    update_local = update_mid.shape[1] // lax.axis_size("row")
    top_local = top_in.shape[0]
    group_id = lax.axis_index("leaf")
    own_half = group_id % 2
    child_slots = parent_slot(rows_low.reshape(2, -1), pivot_local, update_local)
    root_slots = rows_mid.reshape(4, -1) % top_local
    source_order = jnp.bitwise_xor(group_id, jnp.arange(4, dtype=jnp.int32))
    source_slots = jnp.take(root_slots, source_order, axis=0).reshape(-1)
    own_slots = pick_span(child_slots, own_half)
    other_slots = pick_span(child_slots, 1 - own_half)
    low_y = forward_apply(pivot_local_low, low_in.astype(jnp.bfloat16), ())
    low_c = reverse_apply(update_local_low, low_y.astype(jnp.bfloat16)).reshape(2, -1, rhs_width)
    own_part = pick_span(low_c, own_half)
    came_part = partner(pick_span(low_c, 1 - own_half), 0)
    front_rows = jnp.concatenate([mid_in, jnp.zeros((update_local, rhs_width), mid_in.dtype)], 0)
    front_rows = front_rows.at[own_slots].add(-own_part).at[other_slots].add(-came_part)
    mid_y = forward_apply(pivot_mid, front_rows[:pivot_local].astype(jnp.bfloat16), (0,))
    mid_c = front_rows[pivot_local:] - reverse_apply(update_mid, mid_y.astype(jnp.bfloat16))
    spans = mid_c.reshape(4, -1, rhs_width)
    kept_spans = jnp.stack(
        [pick_span(spans, group_id), pick_span(spans, jnp.bitwise_xor(group_id, 2))]
    )
    moved_spans = partner(
        jnp.stack(
            [
                pick_span(spans, jnp.bitwise_xor(group_id, 1)),
                pick_span(spans, jnp.bitwise_xor(group_id, 3)),
            ]
        ),
        0,
    )
    second = partner(jnp.stack([kept_spans[1], moved_spans[1]]), 1)
    arrived = jnp.stack([kept_spans[0], moved_spans[0], second[0], second[1]]).reshape(
        -1, rhs_width
    )
    top_front = top_in.at[source_slots].add(arrived)
    top_y = forward_apply(pivot_top, top_front.astype(jnp.bfloat16), (0, 1))
    top_x = reverse_apply(pivot_top, top_y.astype(jnp.bfloat16))
    asked_rows = top_x[source_slots].reshape(4, -1, rhs_width)
    back_one = partner(jnp.stack([asked_rows[2], asked_rows[3]]), 1)
    back_zero = partner(jnp.stack([asked_rows[1], back_one[1]]), 0)
    by_root = jnp.stack([asked_rows[0], back_zero[0], back_one[0], back_zero[1]])
    mid_above = jnp.take(by_root, source_order, axis=0).reshape(-1, rhs_width)
    mid_sum = forward_apply(update_mid, mid_above.astype(jnp.bfloat16), (0,))
    mid_x = reverse_apply(pivot_mid, (mid_y - mid_sum).astype(jnp.bfloat16))
    front_values = jnp.concatenate([mid_x, mid_above], 0)
    own_rows = front_values[own_slots]
    got_rows = partner(front_values[other_slots], 0)
    low_above = jnp.where(
        own_half == 0,
        jnp.concatenate([own_rows, got_rows], 0),
        jnp.concatenate([got_rows, own_rows], 0),
    )
    low_sum = forward_apply(update_local_low, low_above.astype(jnp.bfloat16), ())
    low_x = reverse_apply(pivot_local_low, (low_y - low_sum).astype(jnp.bfloat16))
    return (
        low_x.reshape(lanczos_low.shape),
        mid_x.reshape(lanczos_mid.shape),
        top_x.reshape(lanczos_top.shape),
    )


def solution(mesh):
    return jax.shard_map(
        body,
        mesh=mesh,
        in_specs=(
            P("leaf", "col", "row", None, None),
            P("leaf", "col", "row", None, None),
            P("leaf", "col", "row", None, None),
            P("leaf", "row", "col"),
            P("leaf", "row", "col"),
            P("row", ("leaf", "col")),
            P("row", ("leaf", "col")),
            P("row", ("leaf", "col")),
            P("leaf", "col", "row", None, None),
            P("leaf", "col", "row", None, None),
        ),
        out_specs=(
            P("leaf", "col", "row", None, None),
            P("leaf", "col", "row", None, None),
            P("leaf", "col", "row", None, None),
        ),
        check_vma=False,
    )
```

```python
import jax
import jax.numpy as jnp
from jax import lax
from jax.sharding import PartitionSpec as P

P1 = 12288


def from_partner(block, axis, bit):
    count = lax.axis_size(axis)
    route = []
    for low in range(count):
        high = low | 1 << bit
        if high != low and high < count:
            route += [(low, high), (high, low)]
    return lax.ppermute(block, axis, route)


def partner(block_data, leaf_bit):
    return from_partner(block_data.astype(jnp.bfloat16), "leaf", leaf_bit).astype(block_data.dtype)


def scatter_sum(block, axis, send_dtype):
    count = lax.axis_size(axis)
    pieces = block.astype(send_dtype).reshape(count, -1, block.shape[-1])
    pieces = lax.all_to_all(pieces, axis, 0, 0, tiled=True)
    return pieces.astype(jnp.float32).sum(0)


def gather_rows(block, axis):
    count = lax.axis_size(axis)
    copies = jnp.broadcast_to(block[None], (count,) + block.shape)
    return lax.all_to_all(copies, axis, 0, 0, tiled=True).reshape(-1, block.shape[-1])


def forward_apply(matrix, vector, leaf_bits):
    gathered = gather_rows(vector, "row")
    result = scatter_sum(
        jnp.dot(matrix, gathered, preferred_element_type=jnp.float32), "col", jnp.bfloat16
    )
    for leaf_bit in leaf_bits:
        result = result + partner(result, leaf_bit)
    return result


def reverse_apply(matrix, vector):
    gathered = gather_rows(vector, "col")
    return scatter_sum(
        lax.dot_general(
            matrix, gathered, (((0,), (0,)), ((), ())), preferred_element_type=jnp.float32
        ),
        "row",
        jnp.bfloat16,
    )


def parent_slot(parent_rows, pivot_local, update_local):
    return jnp.where(
        parent_rows < P1, parent_rows % pivot_local, pivot_local + (parent_rows - P1) % update_local
    )


def pick_span(spans, index_value):
    return lax.dynamic_index_in_dim(spans, index_value, 0, keepdims=False)


def body(
    lanczos_low,
    lanczos_mid,
    lanczos_top,
    pivot_low,
    update_low,
    pivot_mid,
    update_mid,
    pivot_top,
    rows_low,
    rows_mid,
):
    rhs_width = lanczos_low.shape[-1]
    low_in = lanczos_low.reshape(-1, rhs_width)
    mid_in = lanczos_mid.reshape(-1, rhs_width)
    top_in = lanczos_top.reshape(-1, rhs_width)
    pivot_local_low = pivot_low[0]
    update_local_low = update_low[0]
    pivot_local = mid_in.shape[0]
    update_local = update_mid.shape[1] // lax.axis_size("row")
    top_local = top_in.shape[0]
    group_id = lax.axis_index("leaf")
    own_half = group_id % 2
    child_slots = parent_slot(rows_low.reshape(2, -1), pivot_local, update_local)
    root_slots = rows_mid.reshape(4, -1) % top_local
    source_order = jnp.bitwise_xor(group_id, jnp.arange(4, dtype=jnp.int32))
    source_slots = jnp.take(root_slots, source_order, axis=0).reshape(-1)
    own_slots = pick_span(child_slots, own_half)
    other_slots = pick_span(child_slots, 1 - own_half)
    low_y = forward_apply(pivot_local_low, low_in.astype(jnp.bfloat16), ())
    low_c = reverse_apply(update_local_low, low_y.astype(jnp.bfloat16)).reshape(2, -1, rhs_width)
    own_part = pick_span(low_c, own_half)
    came_part = partner(pick_span(low_c, 1 - own_half), 0)
    front_rows = jnp.concatenate([mid_in, jnp.zeros((update_local, rhs_width), mid_in.dtype)], 0)
    front_rows = front_rows.at[own_slots].add(-own_part).at[other_slots].add(-came_part)
    mid_y = forward_apply(pivot_mid, front_rows[:pivot_local].astype(jnp.bfloat16), (0,))
    mid_c = front_rows[pivot_local:] - reverse_apply(update_mid, mid_y.astype(jnp.bfloat16))
    spans = mid_c.reshape(4, -1, rhs_width)
    kept_spans = jnp.stack(
        [pick_span(spans, group_id), pick_span(spans, jnp.bitwise_xor(group_id, 2))]
    )
    moved_spans = partner(
        jnp.stack(
            [
                pick_span(spans, jnp.bitwise_xor(group_id, 1)),
                pick_span(spans, jnp.bitwise_xor(group_id, 3)),
            ]
        ),
        0,
    )
    second = partner(jnp.stack([kept_spans[1], moved_spans[1]]), 1)
    arrived = jnp.stack([kept_spans[0], moved_spans[0], second[0], second[1]]).reshape(
        -1, rhs_width
    )
    top_front = top_in.at[source_slots].add(arrived)
    top_y = forward_apply(pivot_top, top_front.astype(jnp.bfloat16), (0, 1))
    top_x = reverse_apply(pivot_top, top_y.astype(jnp.bfloat16))
    asked_rows = top_x[source_slots].reshape(4, -1, rhs_width)
    back_one = partner(jnp.stack([asked_rows[2], asked_rows[3]]), 1)
    back_zero = partner(jnp.stack([asked_rows[1], back_one[1]]), 0)
    by_root = jnp.stack([asked_rows[0], back_zero[0], back_one[0], back_zero[1]])
    mid_above = jnp.take(by_root, source_order, axis=0).reshape(-1, rhs_width)
    mid_sum = forward_apply(update_mid, mid_above.astype(jnp.bfloat16), (0,))
    mid_x = reverse_apply(pivot_mid, (mid_y - mid_sum).astype(jnp.bfloat16))
    front_values = jnp.concatenate([mid_x, mid_above], 0)
    own_rows = front_values[own_slots]
    got_rows = partner(front_values[other_slots], 0)
    low_above = jnp.where(
        own_half == 0,
        jnp.concatenate([own_rows, got_rows], 0),
        jnp.concatenate([got_rows, own_rows], 0),
    )
    low_sum = forward_apply(update_local_low, low_above.astype(jnp.bfloat16), ())
    low_x = reverse_apply(pivot_local_low, (low_y - low_sum).astype(jnp.bfloat16))
    return (
        low_x.reshape(lanczos_low.shape),
        mid_x.reshape(lanczos_mid.shape),
        top_x.reshape(lanczos_top.shape),
    )


def solution(mesh):
    return jax.shard_map(
        body,
        mesh=mesh,
        in_specs=(
            P("leaf", "col", "row", None, None),
            P("leaf", "col", "row", None, None),
            P("leaf", "col", "row", None, None),
            P("leaf", "row", "col"),
            P("leaf", "row", "col"),
            P("row", ("leaf", "col")),
            P("row", ("leaf", "col")),
            P("row", ("leaf", "col")),
            P("leaf", "col", "row", None, None),
            P("leaf", "col", "row", None, None),
        ),
        out_specs=(
            P("leaf", "col", "row", None, None),
            P("leaf", "col", "row", None, None),
            P("leaf", "col", "row", None, None),
        ),
        check_vma=False,
    )
```

```python
import jax
import jax.numpy as jnp
from jax import lax
from jax.sharding import PartitionSpec as P

P1 = 12288


def from_partner(block, axis, bit):
    count = lax.axis_size(axis)
    route = []
    for low in range(count):
        high = low | 1 << bit
        if high != low and high < count:
            route += [(low, high), (high, low)]
    return lax.ppermute(block, axis, route)


def partner(block_data, leaf_bit):
    return from_partner(block_data.astype(jnp.bfloat16), "leaf", leaf_bit).astype(block_data.dtype)


def scatter_sum(block, axis, send_dtype):
    count = lax.axis_size(axis)
    pieces = block.astype(send_dtype).reshape(count, -1, block.shape[-1])
    pieces = lax.all_to_all(pieces, axis, 0, 0, tiled=True)
    return pieces.astype(jnp.float32).sum(0)


def gather_rows(block, axis):
    count = lax.axis_size(axis)
    copies = jnp.broadcast_to(block[None], (count,) + block.shape)
    return lax.all_to_all(copies, axis, 0, 0, tiled=True).reshape(-1, block.shape[-1])


def forward_apply(matrix, vector, leaf_bits):
    gathered = gather_rows(vector, "row")
    result = scatter_sum(
        jnp.dot(matrix, gathered, preferred_element_type=jnp.float32), "col", jnp.bfloat16
    )
    if len(leaf_bits) == 1:
        result = result + partner(result, leaf_bits[0])
    elif leaf_bits:
        count = lax.axis_size("leaf")
        copies = jnp.broadcast_to(result.astype(jnp.bfloat16)[None], (count,) + result.shape)
        others = lax.all_to_all(copies, "leaf", 0, 0, tiled=True).astype(jnp.float32)
        own = jnp.arange(count) == lax.axis_index("leaf")
        result = result + jnp.where(own[:, None, None], 0.0, others).sum(0)
    return result


def reverse_apply(matrix, vector):
    gathered = gather_rows(vector, "col")
    return scatter_sum(
        lax.dot_general(
            matrix, gathered, (((0,), (0,)), ((), ())), preferred_element_type=jnp.float32
        ),
        "row",
        jnp.bfloat16,
    )


def parent_slot(parent_rows, pivot_local, update_local):
    return jnp.where(
        parent_rows < P1, parent_rows % pivot_local, pivot_local + (parent_rows - P1) % update_local
    )


def pick_span(spans, index_value):
    return lax.dynamic_index_in_dim(spans, index_value, 0, keepdims=False)


def body(
    lanczos_low,
    lanczos_mid,
    lanczos_top,
    pivot_low,
    update_low,
    pivot_mid,
    update_mid,
    pivot_top,
    rows_low,
    rows_mid,
):
    rhs_width = lanczos_low.shape[-1]
    low_in = lanczos_low.reshape(-1, rhs_width)
    mid_in = lanczos_mid.reshape(-1, rhs_width)
    top_in = lanczos_top.reshape(-1, rhs_width)
    pivot_local_low = pivot_low[0]
    update_local_low = update_low[0]
    pivot_local = mid_in.shape[0]
    update_local = update_mid.shape[1] // lax.axis_size("row")
    top_local = top_in.shape[0]
    group_id = lax.axis_index("leaf")
    own_half = group_id % 2
    child_slots = parent_slot(rows_low.reshape(2, -1), pivot_local, update_local)
    root_slots = rows_mid.reshape(4, -1) % top_local
    own_slots = pick_span(child_slots, own_half)
    other_slots = pick_span(child_slots, 1 - own_half)
    low_y = forward_apply(pivot_local_low, low_in.astype(jnp.bfloat16), ())
    low_c = reverse_apply(update_local_low, low_y.astype(jnp.bfloat16)).reshape(2, -1, rhs_width)
    own_part = pick_span(low_c, own_half)
    came_part = partner(pick_span(low_c, 1 - own_half), 0)
    front_rows = jnp.concatenate([mid_in, jnp.zeros((update_local, rhs_width), mid_in.dtype)], 0)
    front_rows = front_rows.at[own_slots].add(-own_part).at[other_slots].add(-came_part)
    mid_y = forward_apply(pivot_mid, front_rows[:pivot_local].astype(jnp.bfloat16), (0,))
    mid_c = front_rows[pivot_local:] - reverse_apply(update_mid, mid_y.astype(jnp.bfloat16))
    spans = mid_c.reshape(4, -1, rhs_width).astype(jnp.bfloat16)
    arrived = lax.all_to_all(spans, "leaf", 0, 0, tiled=True).astype(jnp.float32)
    top_front = top_in.at[root_slots.reshape(-1)].add(arrived.reshape(-1, rhs_width))
    top_y = forward_apply(pivot_top, top_front.astype(jnp.bfloat16), (0, 1))
    top_x = reverse_apply(pivot_top, top_y.astype(jnp.bfloat16))
    asked_rows = top_x[root_slots.reshape(-1)].reshape(4, -1, rhs_width).astype(jnp.bfloat16)
    mid_above = lax.all_to_all(asked_rows, "leaf", 0, 0, tiled=True).astype(jnp.float32)
    mid_above = mid_above.reshape(-1, rhs_width)
    mid_sum = forward_apply(update_mid, mid_above.astype(jnp.bfloat16), (0,))
    mid_x = reverse_apply(pivot_mid, (mid_y - mid_sum).astype(jnp.bfloat16))
    front_values = jnp.concatenate([mid_x, mid_above], 0)
    own_rows = front_values[own_slots]
    got_rows = partner(front_values[other_slots], 0)
    low_above = jnp.where(
        own_half == 0,
        jnp.concatenate([own_rows, got_rows], 0),
        jnp.concatenate([got_rows, own_rows], 0),
    )
    low_sum = forward_apply(update_local_low, low_above.astype(jnp.bfloat16), ())
    low_x = reverse_apply(pivot_local_low, (low_y - low_sum).astype(jnp.bfloat16))
    return (
        low_x.reshape(lanczos_low.shape),
        mid_x.reshape(lanczos_mid.shape),
        top_x.reshape(lanczos_top.shape),
    )


def solution(mesh):
    return jax.shard_map(
        body,
        mesh=mesh,
        in_specs=(
            P("leaf", "col", "row", None, None),
            P("leaf", "col", "row", None, None),
            P("leaf", "col", "row", None, None),
            P("leaf", "row", "col"),
            P("leaf", "row", "col"),
            P("row", ("leaf", "col")),
            P("row", ("leaf", "col")),
            P("row", ("leaf", "col")),
            P("leaf", "col", "row", None, None),
            P("leaf", "col", "row", None, None),
        ),
        out_specs=(
            P("leaf", "col", "row", None, None),
            P("leaf", "col", "row", None, None),
            P("leaf", "col", "row", None, None),
        ),
        check_vma=False,
    )
```

```python
import jax
import jax.numpy as jnp
from jax import lax
from jax.sharding import PartitionSpec as P

P1 = 12288


def from_partner(block, axis, bit):
    count = lax.axis_size(axis)
    route = []
    for low in range(count):
        high = low | 1 << bit
        if high != low and high < count:
            route += [(low, high), (high, low)]
    return lax.ppermute(block, axis, route)


def leaf_exchange(blocks):
    group = lax.axis_index("leaf")
    count = lax.axis_size("leaf")
    came = [pick_span(blocks, group)]
    for step in range(1, count):
        route = [(low, low ^ step) for low in range(count)]
        came.append(lax.ppermute(pick_span(blocks, group ^ step), "leaf", route))
    order = jnp.bitwise_xor(jnp.arange(count, dtype=jnp.int32), group)
    return jnp.take(jnp.stack(came), order, axis=0)


def partner(block_data, leaf_bit):
    return from_partner(block_data.astype(jnp.bfloat16), "leaf", leaf_bit).astype(block_data.dtype)


def scatter_sum(block, axis, send_dtype):
    count = lax.axis_size(axis)
    pieces = block.astype(send_dtype).reshape(count, -1, block.shape[-1])
    pieces = lax.all_to_all(pieces, axis, 0, 0, tiled=True)
    return pieces.astype(jnp.float32).sum(0)


def gather_rows(block, axis):
    count = lax.axis_size(axis)
    copies = jnp.broadcast_to(block[None], (count,) + block.shape)
    return lax.all_to_all(copies, axis, 0, 0, tiled=True).reshape(-1, block.shape[-1])


def forward_apply(matrix, vector, leaf_bits):
    gathered = gather_rows(vector, "row")
    result = scatter_sum(
        jnp.dot(matrix, gathered, preferred_element_type=jnp.float32), "col", jnp.bfloat16
    )
    if len(leaf_bits) == 1:
        result = result + partner(result, leaf_bits[0])
    elif leaf_bits:
        count = lax.axis_size("leaf")
        sent = result.astype(jnp.bfloat16)
        total = result
        for step in range(1, count):
            route = [(low, low ^ step) for low in range(count)]
            total = total + lax.ppermute(sent, "leaf", route).astype(jnp.float32)
        result = total
    return result


def reverse_apply(matrix, vector):
    gathered = gather_rows(vector, "col")
    return scatter_sum(
        lax.dot_general(
            matrix, gathered, (((0,), (0,)), ((), ())), preferred_element_type=jnp.float32
        ),
        "row",
        jnp.bfloat16,
    )


def parent_slot(parent_rows, pivot_local, update_local):
    return jnp.where(
        parent_rows < P1, parent_rows % pivot_local, pivot_local + (parent_rows - P1) % update_local
    )


def pick_span(spans, index_value):
    return lax.dynamic_index_in_dim(spans, index_value, 0, keepdims=False)


def body(
    lanczos_low,
    lanczos_mid,
    lanczos_top,
    pivot_low,
    update_low,
    pivot_mid,
    update_mid,
    pivot_top,
    rows_low,
    rows_mid,
):
    rhs_width = lanczos_low.shape[-1]
    low_in = lanczos_low.reshape(-1, rhs_width)
    mid_in = lanczos_mid.reshape(-1, rhs_width)
    top_in = lanczos_top.reshape(-1, rhs_width)
    pivot_local_low = pivot_low[0]
    update_local_low = update_low[0]
    pivot_local = mid_in.shape[0]
    update_local = update_mid.shape[1] // lax.axis_size("row")
    top_local = top_in.shape[0]
    group_id = lax.axis_index("leaf")
    own_half = group_id % 2
    child_slots = parent_slot(rows_low.reshape(2, -1), pivot_local, update_local)
    root_slots = rows_mid.reshape(4, -1) % top_local
    own_slots = pick_span(child_slots, own_half)
    other_slots = pick_span(child_slots, 1 - own_half)
    low_y = forward_apply(pivot_local_low, low_in.astype(jnp.bfloat16), ())
    low_c = reverse_apply(update_local_low, low_y.astype(jnp.bfloat16)).reshape(2, -1, rhs_width)
    own_part = pick_span(low_c, own_half)
    came_part = partner(pick_span(low_c, 1 - own_half), 0)
    front_rows = jnp.concatenate([mid_in, jnp.zeros((update_local, rhs_width), mid_in.dtype)], 0)
    front_rows = front_rows.at[own_slots].add(-own_part).at[other_slots].add(-came_part)
    mid_y = forward_apply(pivot_mid, front_rows[:pivot_local].astype(jnp.bfloat16), (0,))
    mid_c = front_rows[pivot_local:] - reverse_apply(update_mid, mid_y.astype(jnp.bfloat16))
    spans = mid_c.reshape(4, -1, rhs_width).astype(jnp.bfloat16)
    arrived = leaf_exchange(spans).astype(jnp.float32)
    top_front = top_in.at[root_slots.reshape(-1)].add(arrived.reshape(-1, rhs_width))
    top_y = forward_apply(pivot_top, top_front.astype(jnp.bfloat16), (0, 1))
    top_x = reverse_apply(pivot_top, top_y.astype(jnp.bfloat16))
    asked_rows = top_x[root_slots.reshape(-1)].reshape(4, -1, rhs_width).astype(jnp.bfloat16)
    mid_above = leaf_exchange(asked_rows).astype(jnp.float32)
    mid_above = mid_above.reshape(-1, rhs_width)
    mid_sum = forward_apply(update_mid, mid_above.astype(jnp.bfloat16), (0,))
    mid_x = reverse_apply(pivot_mid, (mid_y - mid_sum).astype(jnp.bfloat16))
    front_values = jnp.concatenate([mid_x, mid_above], 0)
    own_rows = front_values[own_slots]
    got_rows = partner(front_values[other_slots], 0)
    low_above = jnp.where(
        own_half == 0,
        jnp.concatenate([own_rows, got_rows], 0),
        jnp.concatenate([got_rows, own_rows], 0),
    )
    low_sum = forward_apply(update_local_low, low_above.astype(jnp.bfloat16), ())
    low_x = reverse_apply(pivot_local_low, (low_y - low_sum).astype(jnp.bfloat16))
    return (
        low_x.reshape(lanczos_low.shape),
        mid_x.reshape(lanczos_mid.shape),
        top_x.reshape(lanczos_top.shape),
    )


def solution(mesh):
    return jax.shard_map(
        body,
        mesh=mesh,
        in_specs=(
            P("leaf", "col", "row", None, None),
            P("leaf", "col", "row", None, None),
            P("leaf", "col", "row", None, None),
            P("leaf", "row", "col"),
            P("leaf", "row", "col"),
            P("row", ("leaf", "col")),
            P("row", ("leaf", "col")),
            P("row", ("leaf", "col")),
            P("leaf", "col", "row", None, None),
            P("leaf", "col", "row", None, None),
        ),
        out_specs=(
            P("leaf", "col", "row", None, None),
            P("leaf", "col", "row", None, None),
            P("leaf", "col", "row", None, None),
        ),
        check_vma=False,
    )
```

```python
import jax
import jax.numpy as jnp
from jax import lax
from jax.sharding import PartitionSpec as P

P1 = 12288


def from_partner(block, axis, bit):
    count = lax.axis_size(axis)
    route = []
    for low in range(count):
        high = low | 1 << bit
        if high != low and high < count:
            route += [(low, high), (high, low)]
    return lax.ppermute(block, axis, route)


def leaf_exchange(blocks):
    group = lax.axis_index("leaf")
    count = lax.axis_size("leaf")
    near = [(low, low ^ 1) for low in range(count)]
    wrap = [(low, low ^ 3) for low in range(count)]
    first = lax.ppermute(
        jnp.stack([pick_span(blocks, group ^ 1), pick_span(blocks, group ^ 2)]), "leaf", near
    )
    second = lax.ppermute(jnp.stack([pick_span(blocks, group ^ 3), first[1]]), "leaf", wrap)
    came = jnp.stack([pick_span(blocks, group), first[0], second[1], second[0]])
    order = jnp.bitwise_xor(jnp.arange(count, dtype=jnp.int32), group)
    return jnp.take(came, order, axis=0)


def partner(block_data, leaf_bit):
    return from_partner(block_data.astype(jnp.bfloat16), "leaf", leaf_bit).astype(block_data.dtype)


def scatter_sum(block, axis, send_dtype):
    count = lax.axis_size(axis)
    pieces = block.astype(send_dtype).reshape(count, -1, block.shape[-1])
    pieces = lax.all_to_all(pieces, axis, 0, 0, tiled=True)
    return pieces.astype(jnp.float32).sum(0)


def gather_rows(block, axis):
    count = lax.axis_size(axis)
    copies = jnp.broadcast_to(block[None], (count,) + block.shape)
    return lax.all_to_all(copies, axis, 0, 0, tiled=True).reshape(-1, block.shape[-1])


def forward_apply(matrix, vector, leaf_bits):
    gathered = gather_rows(vector, "row")
    result = scatter_sum(
        jnp.dot(matrix, gathered, preferred_element_type=jnp.float32), "col", jnp.bfloat16
    )
    if len(leaf_bits) == 1:
        result = result + partner(result, leaf_bits[0])
    elif leaf_bits:
        count = lax.axis_size("leaf")
        for step in (1, 3):
            route = [(low, low ^ step) for low in range(count)]
            result = result + lax.ppermute(result.astype(jnp.bfloat16), "leaf", route).astype(jnp.float32)
    return result


def reverse_apply(matrix, vector):
    gathered = gather_rows(vector, "col")
    return scatter_sum(
        lax.dot_general(
            matrix, gathered, (((0,), (0,)), ((), ())), preferred_element_type=jnp.float32
        ),
        "row",
        jnp.bfloat16,
    )


def parent_slot(parent_rows, pivot_local, update_local):
    return jnp.where(
        parent_rows < P1, parent_rows % pivot_local, pivot_local + (parent_rows - P1) % update_local
    )


def pick_span(spans, index_value):
    return lax.dynamic_index_in_dim(spans, index_value, 0, keepdims=False)


def body(
    lanczos_low,
    lanczos_mid,
    lanczos_top,
    pivot_low,
    update_low,
    pivot_mid,
    update_mid,
    pivot_top,
    rows_low,
    rows_mid,
):
    rhs_width = lanczos_low.shape[-1]
    low_in = lanczos_low.reshape(-1, rhs_width)
    mid_in = lanczos_mid.reshape(-1, rhs_width)
    top_in = lanczos_top.reshape(-1, rhs_width)
    pivot_local_low = pivot_low[0]
    update_local_low = update_low[0]
    pivot_local = mid_in.shape[0]
    update_local = update_mid.shape[1] // lax.axis_size("row")
    top_local = top_in.shape[0]
    group_id = lax.axis_index("leaf")
    own_half = group_id % 2
    child_slots = parent_slot(rows_low.reshape(2, -1), pivot_local, update_local)
    root_slots = rows_mid.reshape(4, -1) % top_local
    own_slots = pick_span(child_slots, own_half)
    other_slots = pick_span(child_slots, 1 - own_half)
    low_y = forward_apply(pivot_local_low, low_in.astype(jnp.bfloat16), ())
    low_c = reverse_apply(update_local_low, low_y.astype(jnp.bfloat16)).reshape(2, -1, rhs_width)
    own_part = pick_span(low_c, own_half)
    came_part = partner(pick_span(low_c, 1 - own_half), 0)
    front_rows = jnp.concatenate([mid_in, jnp.zeros((update_local, rhs_width), mid_in.dtype)], 0)
    front_rows = front_rows.at[own_slots].add(-own_part).at[other_slots].add(-came_part)
    mid_y = forward_apply(pivot_mid, front_rows[:pivot_local].astype(jnp.bfloat16), (0,))
    mid_c = front_rows[pivot_local:] - reverse_apply(update_mid, mid_y.astype(jnp.bfloat16))
    spans = mid_c.reshape(4, -1, rhs_width).astype(jnp.bfloat16)
    arrived = leaf_exchange(spans).astype(jnp.float32)
    top_front = top_in.at[root_slots.reshape(-1)].add(arrived.reshape(-1, rhs_width))
    top_y = forward_apply(pivot_top, top_front.astype(jnp.bfloat16), (0, 1))
    top_x = reverse_apply(pivot_top, top_y.astype(jnp.bfloat16))
    asked_rows = top_x[root_slots.reshape(-1)].reshape(4, -1, rhs_width).astype(jnp.bfloat16)
    mid_above = leaf_exchange(asked_rows).astype(jnp.float32)
    mid_above = mid_above.reshape(-1, rhs_width)
    mid_sum = forward_apply(update_mid, mid_above.astype(jnp.bfloat16), (0,))
    mid_x = reverse_apply(pivot_mid, (mid_y - mid_sum).astype(jnp.bfloat16))
    front_values = jnp.concatenate([mid_x, mid_above], 0)
    own_rows = front_values[own_slots]
    got_rows = partner(front_values[other_slots], 0)
    low_above = jnp.where(
        own_half == 0,
        jnp.concatenate([own_rows, got_rows], 0),
        jnp.concatenate([got_rows, own_rows], 0),
    )
    low_sum = forward_apply(update_local_low, low_above.astype(jnp.bfloat16), ())
    low_x = reverse_apply(pivot_local_low, (low_y - low_sum).astype(jnp.bfloat16))
    return (
        low_x.reshape(lanczos_low.shape),
        mid_x.reshape(lanczos_mid.shape),
        top_x.reshape(lanczos_top.shape),
    )


def solution(mesh):
    return jax.shard_map(
        body,
        mesh=mesh,
        in_specs=(
            P("leaf", "col", "row", None, None),
            P("leaf", "col", "row", None, None),
            P("leaf", "col", "row", None, None),
            P("leaf", "row", "col"),
            P("leaf", "row", "col"),
            P("row", ("leaf", "col")),
            P("row", ("leaf", "col")),
            P("row", ("leaf", "col")),
            P("leaf", "col", "row", None, None),
            P("leaf", "col", "row", None, None),
        ),
        out_specs=(
            P("leaf", "col", "row", None, None),
            P("leaf", "col", "row", None, None),
            P("leaf", "col", "row", None, None),
        ),
        check_vma=False,
    )
```
